512 devices in a mesh: chan: 4 (over x), tile: 128 (over z, y, core).
Axes of the slice: x: 4, y: 8, z: 8, core: 2. Of those that a mesh axis runs over, the one named last changes fastest.
Arguments:
- visibilities: bfloat16 [131072, 1024], P('tile', 'chan'), parts along dimension 1, may hold values from -6 to 6
- send_list: int32 [65536, 8], P(('chan', 'tile')), parts along dimension 0, may hold values from -1 to 1023, as said below
- pixels: int32 [2, 524288], P(None, ('chan', 'tile')), parts along dimension 1, may hold values from 0 to 31
- offsets: int32 [2, 524288], P(None, ('chan', 'tile')), parts along dimension 1, may hold values from 0 to 15
- taper: float32 [8, 16], replicated, may hold values from 0.1 to 0.6
Outputs:
- tiles: float32 [128, 32, 32, 1024], P('tile', None, None, 'chan'), parts along dimension 3
The draws below stay inside these ranges and needn't reach their ends.
There are 4 independent parts, one for each index of `chan`. The reference program is written for one: setup_inputs(seed, part) draws one part's arguments, and reference() takes and returns one part's arrays. A program takes and returns all parts, laid end to end along the dimension named above; an argument that names none is the same for every part. Nothing has to cross between parts.
Inputs may be any that keep to these rules, and one draw needn't show every extreme that they name: `send_list`: for every sender and tile the live entries come first and are distinct local row indices; no row is listed twice by one sender; the rest are -1. One tile, drawn from the seed, gets 8 live slots from every sender, and every sender lists its last row.
All inputs are finite; a program needn't handle non-finite values.
Results may differ from the reference program's by a relative error of at most 0.0029.
Values may be sent and summed in bfloat16 or wider, within the bound.
No kernel may reach another device: no remote copies, remote signals or barrier semaphores. Data moves between devices by JAX's collectives and lax.ppermute only.
A program may use at most 64 MiB of HBM per device.

```python
import jax
import jax.numpy as jnp
from jax import lax

CH = 128
TS = 32
ROWS_DEV = 1024
TAPS = 8
OS = 16
TILES_Y = 8
TILES_X = 16
CAP = 8
ROWS_ALL = 131072
N_TILE = 128


def draw_send_list(key, part):
    center_key = jax.random.fold_in(key, 7001)
    center_x = jax.random.randint(jax.random.fold_in(center_key, 1), (), 0, N_TILE // TILES_Y)
    center_y = jax.random.randint(jax.random.fold_in(center_key, 2), (), 0, TILES_Y)
    tile_ids = jnp.arange(N_TILE, dtype=jnp.int32)
    distance = (tile_ids // TILES_Y - center_x) ** 2 + (tile_ids % TILES_Y - center_y) ** 2
    reach = 2 * N_TILE
    slot_ids = jnp.arange(CAP, dtype=jnp.int32)

    def one_sender(sender):
        sender_key = jax.random.fold_in(key, sender + 100)
        jitter = jax.random.randint(jax.random.fold_in(sender_key, 1), (N_TILE,), 0, CAP // 2 + 1)
        jitter = jnp.where(distance > 0, jitter, 0)
        counts = jnp.clip(CAP - distance * CAP // reach - jitter, 0, CAP)
        ordering = jax.random.permutation(jax.random.fold_in(sender_key, 2), ROWS_DEV).astype(jnp.int32)
        leading = ordering[0]
        ordering = jnp.where(ordering == ROWS_DEV - 1, leading, ordering).at[0].set(ROWS_DEV - 1)
        starts = jnp.cumsum(counts) - counts
        chosen = ordering[jnp.clip(starts[:, None] + slot_ids[None, :], 0, ROWS_DEV - 1)]
        return jnp.where(slot_ids[None, :] < counts[:, None], chosen, -1)
    listed = jax.vmap(one_sender)(jnp.arange(N_TILE, dtype=jnp.int32))
    return listed.reshape(N_TILE * N_TILE, CAP).astype(jnp.int32)


def set_ends(array, stream_key, low, high):
    dims = array.shape
    spot = [jax.random.randint(jax.random.fold_in(stream_key, axis), (), 0, dims[axis]) for axis in range(len(dims))]
    array = array.at[tuple(spot)].set(low)
    longest = dims.index(max(dims))
    spot[longest] = (spot[longest] + 1) % dims[longest]
    return array.at[tuple(spot)].set(high)


def block_scale(key, dims, split, low, largest):
    def one(position, shards_of):
        draws = jax.random.uniform(jax.random.fold_in(jax.random.fold_in(key, 6), position), (shards_of,), jnp.float32, low / len(split), largest / len(split))
        return jnp.repeat(jnp.exp(draws), dims[position] // shards_of).reshape((-1,) + (1,) * (len(dims) - position - 1))

    gain = one(*split[0])
    for cut in split[1:]:
        gain = gain * one(*cut)
    return gain


def normal_values(stream_key, extent, spread, most, pieces=(), held_as=jnp.bfloat16):
    gain = block_scale(stream_key, extent, pieces, -0.22, 0.18) if pieces else 1.0
    values = jax.random.normal(stream_key, extent, jnp.float32) * spread * gain
    return jnp.minimum(jnp.maximum(values, -most), most).astype(held_as)


def setup_inputs(seed: int = 0, part: int = 0) -> dict:
    key_list = jax.random.split(jax.random.key(seed), 6)
    own_keys = jax.random.split(jax.random.fold_in(key_list[5], part), 6)
    return {
        "visibilities": normal_values(own_keys[0], (ROWS_ALL, 2 * CH), 1.0, 6.0, ((0, 128),)),
        "send_list": draw_send_list(jax.random.fold_in(jax.random.fold_in(key_list[5], part), 71), part),
        "pixels": set_ends(jax.random.randint(own_keys[2], (2, ROWS_ALL), 0, TS), jax.random.fold_in(own_keys[2], 1), 0, TS - 1).astype(jnp.int32),
        "offsets": set_ends(jax.random.randint(own_keys[3], (2, ROWS_ALL), 0, OS), jax.random.fold_in(own_keys[3], 1), 0, OS - 1).astype(jnp.int32),
        "taper": jnp.clip(jax.random.uniform(key_list[4], (TAPS, OS), jnp.float32, 0.1, 0.6), 0.1, 0.6),
    }


def reference(visibilities, send_list, pixels, offsets, taper):
    components = visibilities.shape[1]
    width_x = TILES_X * TS + 8
    width_y = TILES_Y * TS + 8
    slot_total = N_TILE * CAP
    destination = jnp.arange(slot_total, dtype=jnp.int32) // CAP
    base_x = (destination // TILES_Y) * TS
    base_y = (destination % TILES_Y) * TS
    tap_index = jnp.arange(TAPS, dtype=jnp.int32)

    def per_sender(canvas, sender):
        listed = lax.dynamic_slice_in_dim(send_list, (sender * N_TILE).astype(jnp.int32), N_TILE, 0).reshape(-1)
        is_live = listed >= 0
        picked = (jnp.where(is_live, listed, 0) + sender * ROWS_DEV).astype(jnp.int32)
        slot_rows = jnp.take(visibilities, picked, axis=0).astype(jnp.float32) * is_live[:, None].astype(jnp.float32)
        kernel_u = jnp.take(taper, jnp.take(offsets[0], picked), axis=1)
        kernel_v = jnp.take(taper, jnp.take(offsets[1], picked), axis=1)
        weights = lax.optimization_barrier((kernel_u[:, None, :] * kernel_v[None, :, :]).astype(jnp.bfloat16))
        weights = weights.astype(jnp.float32)
        pos_x = base_x + jnp.take(pixels[0], picked)
        pos_y = base_y + jnp.take(pixels[1], picked)
        for tap_u in range(TAPS):
            flat_index = ((pos_x + tap_u)[None, :] * width_y + pos_y[None, :] + tap_index[:, None]).reshape(-1)
            values = (weights[tap_u][:, :, None] * slot_rows[None, :, :]).reshape(-1, components)
            canvas = canvas.at[flat_index].add(values)
        return canvas, None

    canvas = jnp.zeros((width_x * width_y, components), jnp.float32)
    canvas, _ = lax.scan(per_sender, canvas, jnp.arange(N_TILE, dtype=jnp.int32))
    grid = canvas.reshape(width_x, width_y, components)[4:width_x - 4, 4:width_y - 4]
    grid = grid.reshape(TILES_X, TS, TILES_Y, TS, components).transpose(0, 2, 1, 3, 4)
    return grid.reshape(N_TILE, TS, TS, components)
```

```python
import jax
import jax.numpy as jnp
from jax import lax
from jax.sharding import PartitionSpec as P

TS = 32
TILES_Y = 8
META = 4


def passed_along(value, axis, by):
    count = lax.axis_size(axis)
    pairs = [(i, i + by) for i in range(count) if 0 <= i + by < count]
    return lax.ppermute(value, axis, pairs)


def spread(kernel, pixel, padded_side):
    cell_index = jnp.arange(padded_side, dtype=jnp.int32)[:, None] - pixel[None, :]
    tap_index = jnp.arange(kernel.shape[0], dtype=jnp.int32)[:, None, None]
    return jnp.sum(jnp.where(cell_index[None] == tap_index, kernel[:, None, :], 0.0), axis=0)


def place_block(block_rows, block_meta, taper, padded_side):
    levels = jnp.arange(taper.shape[1], dtype=jnp.int32)[:, None]
    select_u = (levels == block_meta[2][None, :]).astype(jnp.float32)
    select_v = (levels == block_meta[3][None, :]).astype(jnp.float32)
    kernel_u = jnp.dot(
        taper, select_u, precision=lax.Precision.HIGHEST, preferred_element_type=jnp.float32
    )
    kernel_v = jnp.dot(
        taper, select_v, precision=lax.Precision.HIGHEST, preferred_element_type=jnp.float32
    )
    spread_u = spread(kernel_u, block_meta[0], padded_side)
    spread_v = spread(kernel_v, block_meta[1], padded_side)
    weights = (spread_u[:, None, :] * spread_v[None, :, :]).astype(jnp.bfloat16)
    weights = weights.reshape(padded_side * padded_side, -1)
    return jnp.dot(weights, block_rows, preferred_element_type=jnp.float32)


def grid_blocks(slot_rows, slot_meta, taper, padded_side, block_size, block_count):
    width = slot_rows.shape[1]

    def one_block(index, running):
        start = index * block_size
        block_rows = lax.dynamic_slice_in_dim(slot_rows, start, block_size, 0)
        block_meta = lax.dynamic_slice_in_dim(slot_meta, start, block_size, 1)
        return running + place_block(block_rows, block_meta, taper, padded_side)

    initial = jnp.zeros((padded_side * padded_side, width), jnp.float32)
    return lax.fori_loop(0, block_count, one_block, initial)


def body(visibilities, send_list, pixels, offsets, taper):
    tile_count = lax.axis_size("tile")
    slot_cap = send_list.shape[1]
    rows_dev, components = visibilities.shape
    padded_side = TS + 8
    slot_total = tile_count * slot_cap
    block_size = min(512, slot_total)

    listed = send_list.reshape(-1)
    row_ids = jnp.arange(rows_dev, dtype=jnp.int32)
    chosen = (listed[:, None] == row_ids[None, :]).astype(jnp.bfloat16)
    outgoing = jnp.dot(chosen, visibilities, preferred_element_type=jnp.float32)
    outgoing = outgoing.astype(jnp.bfloat16)
    meta_src = jnp.concatenate([pixels, offsets], 0).astype(jnp.bfloat16)
    slot_meta = lax.dot_general(
        chosen, meta_src, (((1,), (1,)), ((), ())), preferred_element_type=jnp.float32
    ).astype(jnp.bfloat16)
    packed = jnp.concatenate(
        [
            outgoing.reshape(tile_count, slot_cap * components),
            slot_meta.reshape(tile_count, slot_cap * META),
        ],
        1,
    )
    arrived = lax.all_to_all(packed, "tile", split_axis=0, concat_axis=0, tiled=True)
    arrived_rows = arrived[:, : slot_cap * components].reshape(slot_total, components)
    meta_rows = (
        arrived[:, slot_cap * components :]
        .reshape(slot_total, META)
        .astype(jnp.int32)
        .transpose(1, 0)
    )
    padded_grid = grid_blocks(
        arrived_rows,
        meta_rows,
        taper,
        padded_side,
        block_size,
        slot_total // block_size,
    )
    grid = padded_grid.reshape(padded_side, padded_side, components)

    from_below = passed_along(grid[0:4], "tile", -TILES_Y)
    from_above = passed_along(grid[TS + 4 : TS + 8], "tile", TILES_Y)
    grid = grid.at[TS : TS + 4].add(from_below)
    grid = grid.at[4:8].add(from_above)
    tile_row = lax.axis_index("tile") % TILES_Y
    inner = grid[4 : TS + 4]
    from_next = passed_along(inner[:, 0:4], "tile", -1)
    from_prev = passed_along(inner[:, TS + 4 : TS + 8], "tile", 1)
    from_next = jnp.where(tile_row + 1 < TILES_Y, from_next, 0.0)
    from_prev = jnp.where(tile_row >= 1, from_prev, 0.0)
    result = inner[:, 4 : TS + 4]
    result = result.at[:, TS - 4 : TS].add(from_next)
    result = result.at[:, 0:4].add(from_prev)
    return result[None]


def solution(mesh):
    placed = (
        P("tile", "chan"),
        P(("chan", "tile"), None),
        P(None, ("chan", "tile")),
        P(None, ("chan", "tile")),
        P(),
    )
    return jax.shard_map(
        body, mesh=mesh, in_specs=placed, out_specs=P("tile", None, None, "chan"), check_vma=False
    )
```

```python
import jax
import jax.numpy as jnp
from jax import lax
from jax.sharding import PartitionSpec as P

TS = 32
TILES_Y = 8
META = 4


def passed_along(value, axis, by):
    count = lax.axis_size(axis)
    pairs = [(i, i + by) for i in range(count) if 0 <= i + by < count]
    return lax.ppermute(value, axis, pairs)


def spread(kernel, pixel, padded_side):
    cell_index = jnp.arange(padded_side, dtype=jnp.int32)[:, None] - pixel[None, :]
    tap_index = jnp.arange(kernel.shape[0], dtype=jnp.int32)[:, None, None]
    return jnp.sum(jnp.where(cell_index[None] == tap_index, kernel[:, None, :], 0.0), axis=0)


def place_block(block_rows, block_meta, taper, padded_side):
    levels = jnp.arange(taper.shape[1], dtype=jnp.int32)[:, None]
    select_u = (levels == block_meta[2][None, :]).astype(jnp.float32)
    select_v = (levels == block_meta[3][None, :]).astype(jnp.float32)
    kernel_u = jnp.dot(
        taper, select_u, precision=lax.Precision.HIGHEST, preferred_element_type=jnp.float32
    )
    kernel_v = jnp.dot(
        taper, select_v, precision=lax.Precision.HIGHEST, preferred_element_type=jnp.float32
    )
    spread_u = spread(kernel_u, block_meta[0], padded_side)
    spread_v = spread(kernel_v, block_meta[1], padded_side)
    weights = (spread_u[:, None, :] * spread_v[None, :, :]).astype(jnp.bfloat16)
    weights = weights.reshape(padded_side * padded_side, -1)
    return jnp.dot(weights, block_rows, preferred_element_type=jnp.float32)


def grid_blocks(slot_rows, slot_meta, taper, padded_side, block_size, block_count):
    width = slot_rows.shape[1]

    def one_block(index, running):
        start = index * block_size
        block_rows = lax.dynamic_slice_in_dim(slot_rows, start, block_size, 0)
        block_meta = lax.dynamic_slice_in_dim(slot_meta, start, block_size, 1)
        return running + place_block(block_rows, block_meta, taper, padded_side)

    initial = jnp.zeros((padded_side * padded_side, width), jnp.float32)
    return lax.fori_loop(0, block_count, one_block, initial)


def body(visibilities, send_list, pixels, offsets, taper):
    tile_count = lax.axis_size("tile")
    slot_cap = send_list.shape[1]
    rows_dev, components = visibilities.shape
    padded_side = TS + 8
    slot_total = tile_count * slot_cap
    block_size = min(512, slot_total)
    meta_lanes = 128

    listed = send_list.transpose(1, 0).reshape(-1)
    row_ids = jnp.arange(rows_dev, dtype=jnp.int32)
    chosen = (listed[:, None] == row_ids[None, :]).astype(jnp.bfloat16)
    outgoing = jnp.dot(chosen, visibilities, preferred_element_type=jnp.float32)
    outgoing = outgoing.astype(jnp.bfloat16)
    meta_src = jnp.concatenate([pixels, offsets], 0).astype(jnp.bfloat16)
    slot_meta = lax.dot_general(
        meta_src, chosen, (((1,), (1,)), ((), ())), preferred_element_type=jnp.float32
    )
    slot_meta = slot_meta.reshape(META, slot_cap, tile_count).transpose(2, 1, 0)
    slot_meta = slot_meta.reshape(tile_count, slot_cap * META).astype(jnp.bfloat16)
    slot_meta = jnp.pad(slot_meta, ((0, 0), (0, meta_lanes - slot_cap * META)))
    packed = jnp.concatenate(
        [outgoing[k * tile_count : (k + 1) * tile_count] for k in range(slot_cap)] + [slot_meta],
        1,
    )
    arrived = lax.all_to_all(packed, "tile", split_axis=0, concat_axis=0, tiled=True)
    arrived_rows = jnp.concatenate(
        [arrived[:, k * components : (k + 1) * components] for k in range(slot_cap)], 0
    )
    meta_rows = arrived[:, slot_cap * components : slot_cap * components + slot_cap * META]
    meta_rows = meta_rows.astype(jnp.int32).reshape(tile_count, slot_cap, META)
    meta_rows = meta_rows.transpose(2, 1, 0).reshape(META, slot_total)
    padded_grid = grid_blocks(
        arrived_rows,
        meta_rows,
        taper,
        padded_side,
        block_size,
        slot_total // block_size,
    )
    grid = padded_grid.reshape(padded_side, padded_side, components)

    from_below = passed_along(grid[0:4].astype(jnp.bfloat16), "tile", -TILES_Y)
    from_above = passed_along(grid[TS + 4 : TS + 7].astype(jnp.bfloat16), "tile", TILES_Y)
    grid = grid.at[TS : TS + 4].add(from_below.astype(jnp.float32))
    grid = grid.at[4:7].add(from_above.astype(jnp.float32))
    tile_row = lax.axis_index("tile") % TILES_Y
    inner = grid[4 : TS + 4]
    from_next = passed_along(inner[:, 0:4], "tile", -1)
    from_prev = passed_along(inner[:, TS + 4 : TS + 7], "tile", 1)
    from_next = jnp.where(tile_row + 1 < TILES_Y, from_next, 0.0)
    from_prev = jnp.where(tile_row >= 1, from_prev, 0.0)
    result = inner[:, 4 : TS + 4]
    result = result.at[:, TS - 4 : TS].add(from_next)
    result = result.at[:, 0:3].add(from_prev)
    return result[None]


def solution(mesh):
    placed = (
        P("tile", "chan"),
        P(("chan", "tile"), None),
        P(None, ("chan", "tile")),
        P(None, ("chan", "tile")),
        P(),
    )
    return jax.shard_map(
        body, mesh=mesh, in_specs=placed, out_specs=P("tile", None, None, "chan"), check_vma=False
    )
```

```python
import jax
import jax.numpy as jnp
from jax import lax
from jax.sharding import PartitionSpec as P

TS = 32
TILES_Y = 8
META = 4


def passed_along(value, axis, by):
    count = lax.axis_size(axis)
    pairs = [(i, i + by) for i in range(count) if 0 <= i + by < count]
    return lax.ppermute(value, axis, pairs)


def spread(kernel, pixel, padded_side):
    cell_index = jnp.arange(padded_side, dtype=jnp.int32)[:, None] - pixel[None, :]
    tap_index = jnp.arange(kernel.shape[0], dtype=jnp.int32)[:, None, None]
    return jnp.sum(jnp.where(cell_index[None] == tap_index, kernel[:, None, :], 0.0), axis=0)


def kernel_of(taper, offset):
    levels = jnp.arange(taper.shape[1], dtype=jnp.int32)[:, None]
    select = (levels == offset[None, :]).astype(jnp.float32)
    return jnp.dot(taper, select, precision=lax.Precision.HIGHEST, preferred_element_type=jnp.float32)


def place_rows(spread_u, spread_v, slot_rows):
    weights = (spread_u[:, None, :] * spread_v[None, :, :]).astype(jnp.bfloat16)
    weights = weights.reshape(spread_u.shape[0] * spread_v.shape[0], -1)
    cells = jnp.dot(weights, slot_rows, preferred_element_type=jnp.float32)
    return cells.reshape(spread_u.shape[0], spread_v.shape[0], -1)


def body(visibilities, send_list, pixels, offsets, taper):
    tile_count = lax.axis_size("tile")
    slot_cap = send_list.shape[1]
    rows_dev, components = visibilities.shape
    padded_side = TS + 8
    slot_total = tile_count * slot_cap
    halves = 2
    per_half = slot_cap // halves
    half_lanes = per_half * components + 128

    listed = send_list.transpose(1, 0).reshape(-1)
    row_ids = jnp.arange(rows_dev, dtype=jnp.int32)
    chosen = (listed[:, None] == row_ids[None, :]).astype(jnp.bfloat16)
    outgoing = jnp.dot(chosen, visibilities, preferred_element_type=jnp.float32)
    outgoing = outgoing.astype(jnp.bfloat16)
    meta_src = jnp.concatenate([pixels, offsets], 0).astype(jnp.bfloat16)
    slot_meta = lax.dot_general(
        meta_src, chosen, (((1,), (1,)), ((), ())), preferred_element_type=jnp.float32
    )
    slot_meta = slot_meta.reshape(META, slot_cap, tile_count).transpose(2, 1, 0)
    slot_meta = slot_meta.reshape(tile_count, slot_cap * META).astype(jnp.bfloat16)
    pad = half_lanes - per_half * components
    tails = [
        jnp.pad(slot_meta, ((0, 0), (0, pad - slot_cap * META))),
        jnp.zeros((tile_count, pad), jnp.bfloat16),
    ]
    packed = jnp.stack(
        [
            jnp.concatenate(
                [
                    outgoing[(h * per_half + j) * tile_count : (h * per_half + j + 1) * tile_count]
                    for j in range(per_half)
                ]
                + [tails[h]],
                1,
            )
            for h in range(halves)
        ],
        1,
    )
    arrived = lax.all_to_all(packed, "tile", split_axis=0, concat_axis=0, tiled=True)
    arrived_rows = jnp.concatenate(
        [
            arrived[:, h, j * components : (j + 1) * components]
            for h in range(halves)
            for j in range(per_half)
        ],
        0,
    )
    meta_rows = arrived[:, 0, per_half * components : per_half * components + slot_cap * META]
    meta_rows = meta_rows.astype(jnp.int32).reshape(tile_count, slot_cap, META)
    meta_rows = meta_rows.transpose(2, 1, 0).reshape(META, slot_total)

    spread_u = spread(kernel_of(taper, meta_rows[2]), meta_rows[0], padded_side)
    spread_v = spread(kernel_of(taper, meta_rows[3]), meta_rows[1], padded_side)
    low = place_rows(spread_u[0:4], spread_v, arrived_rows)
    high = place_rows(spread_u[TS + 4 : TS + 7], spread_v, arrived_rows)

    from_below = passed_along(low.astype(jnp.bfloat16), "tile", -TILES_Y)
    from_above = passed_along(high.astype(jnp.bfloat16), "tile", TILES_Y)
    inner = place_rows(spread_u[4 : TS + 4], spread_v, arrived_rows)
    inner = inner.at[TS - 4 : TS].add(from_below.astype(jnp.float32))
    inner = inner.at[0:3].add(from_above.astype(jnp.float32))
    tile_row = lax.axis_index("tile") % TILES_Y
    from_next = passed_along(inner[:, 0:4], "tile", -1)
    from_prev = passed_along(inner[:, TS + 4 : TS + 7], "tile", 1)
    from_next = jnp.where(tile_row + 1 < TILES_Y, from_next, 0.0)
    from_prev = jnp.where(tile_row >= 1, from_prev, 0.0)
    result = inner[:, 4 : TS + 4]
    result = result.at[:, TS - 4 : TS].add(from_next)
    result = result.at[:, 0:3].add(from_prev)
    return result[None]


def solution(mesh):
    placed = (
        P("tile", "chan"),
        P(("chan", "tile"), None),
        P(None, ("chan", "tile")),
        P(None, ("chan", "tile")),
        P(),
    )
    return jax.shard_map(
        body, mesh=mesh, in_specs=placed, out_specs=P("tile", None, None, "chan"), check_vma=False
    )
```

```python
import jax
import jax.numpy as jnp
from jax import lax
from jax.sharding import PartitionSpec as P

TS = 32
TILES_Y = 8
META = 4


def passed_along(value, axis, by):
    count = lax.axis_size(axis)
    pairs = [(i, i + by) for i in range(count) if 0 <= i + by < count]
    return lax.ppermute(value, axis, pairs)


def spread(kernel, pixel, padded_side):
    cell_index = jnp.arange(padded_side, dtype=jnp.int32)[:, None] - pixel[None, :]
    tap_index = jnp.arange(kernel.shape[0], dtype=jnp.int32)[:, None, None]
    return jnp.sum(jnp.where(cell_index[None] == tap_index, kernel[:, None, :], 0.0), axis=0)


def kernel_of(taper, offset):
    levels = jnp.arange(taper.shape[1], dtype=jnp.int32)[:, None]
    select = (levels == offset[None, :]).astype(jnp.float32)
    return jnp.dot(taper, select, precision=lax.Precision.HIGHEST, preferred_element_type=jnp.float32)


def place_rows(spread_u, spread_v, slot_rows):
    weights = (spread_u[:, None, :] * spread_v[None, :, :]).astype(jnp.bfloat16)
    weights = weights.reshape(spread_u.shape[0] * spread_v.shape[0], -1)
    cells = jnp.dot(weights, slot_rows, preferred_element_type=jnp.float32)
    return cells.reshape(spread_u.shape[0], spread_v.shape[0], -1)


def body(visibilities, send_list, pixels, offsets, taper):
    tile_count = lax.axis_size("tile")
    slot_cap = send_list.shape[1]
    rows_dev, components = visibilities.shape
    padded_side = TS + 8
    slot_total = tile_count * slot_cap
    halves = 2
    per_half = slot_cap // halves
    half_lanes = per_half * components + 128

    listed = send_list.transpose(1, 0).reshape(-1)
    row_ids = jnp.arange(rows_dev, dtype=jnp.int32)
    chosen = (listed[:, None] == row_ids[None, :]).astype(jnp.bfloat16)
    outgoing = jnp.dot(chosen, visibilities, preferred_element_type=jnp.float32)
    outgoing = outgoing.astype(jnp.bfloat16)
    meta_src = jnp.concatenate([pixels, offsets], 0).astype(jnp.bfloat16)
    slot_meta = lax.dot_general(
        meta_src, chosen, (((1,), (1,)), ((), ())), preferred_element_type=jnp.float32
    )
    slot_meta = slot_meta.reshape(META, slot_cap, tile_count).transpose(2, 1, 0)
    slot_meta = slot_meta.reshape(tile_count, slot_cap * META).astype(jnp.bfloat16)
    pad = half_lanes - per_half * components
    tails = [
        jnp.pad(slot_meta, ((0, 0), (0, pad - slot_cap * META))),
        jnp.zeros((tile_count, pad), jnp.bfloat16),
    ]
    packed = jnp.stack(
        [
            jnp.concatenate(
                [
                    outgoing[(h * per_half + j) * tile_count : (h * per_half + j + 1) * tile_count]
                    for j in range(per_half)
                ]
                + [tails[h]],
                1,
            )
            for h in range(halves)
        ],
        1,
    )
    arrived = lax.all_to_all(packed, "tile", split_axis=0, concat_axis=0, tiled=True)
    arrived_rows = jnp.concatenate(
        [
            arrived[:, h, j * components : (j + 1) * components]
            for h in range(halves)
            for j in range(per_half)
        ],
        0,
    )
    meta_rows = arrived[:, 0, per_half * components : per_half * components + slot_cap * META]
    meta_rows = meta_rows.astype(jnp.int32).reshape(tile_count, slot_cap, META)
    meta_rows = meta_rows.transpose(2, 1, 0).reshape(META, slot_total)

    spread_u = spread(kernel_of(taper, meta_rows[2]), meta_rows[0], padded_side)
    spread_v = spread(kernel_of(taper, meta_rows[3]), meta_rows[1], padded_side)
    source = {-1: (TS + 4, 3), 0: (4, TS), 1: (0, 4)}
    target = {-1: 0, 0: 0, 1: TS - 4}
    tile_row = lax.axis_index("tile") % TILES_Y
    pieces = {}
    for step_x in (-1, 0, 1):
        for step_y in (-1, 0, 1):
            if step_x == 0 and step_y == 0:
                continue
            rows_from, rows_span = source[step_x]
            cols_from, cols_span = source[step_y]
            piece = place_rows(
                spread_u[rows_from : rows_from + rows_span],
                spread_v[cols_from : cols_from + cols_span],
                arrived_rows,
            )
            if step_x != 0:
                piece = piece.astype(jnp.bfloat16)
            pieces[step_x, step_y] = passed_along(piece, "tile", -(step_x * TILES_Y + step_y))
    result = place_rows(spread_u[4 : TS + 4], spread_v[4 : TS + 4], arrived_rows)
    for (step_x, step_y), incoming in pieces.items():
        inside = (tile_row + step_y >= 0) & (tile_row + step_y < TILES_Y)
        incoming = jnp.where(inside, incoming.astype(jnp.float32), 0.0)
        rows_at, cols_at = target[step_x], target[step_y]
        result = result.at[
            rows_at : rows_at + incoming.shape[0], cols_at : cols_at + incoming.shape[1]
        ].add(incoming)
    return result[None]


def solution(mesh):
    placed = (
        P("tile", "chan"),
        P(("chan", "tile"), None),
        P(None, ("chan", "tile")),
        P(None, ("chan", "tile")),
        P(),
    )
    return jax.shard_map(
        body, mesh=mesh, in_specs=placed, out_specs=P("tile", None, None, "chan"), check_vma=False
    )
```

```python
import jax
import jax.numpy as jnp
from jax import lax
from jax.sharding import PartitionSpec as P

TS = 32
TILES_Y = 8
META = 4


def passed_along(value, axis, by):
    count = lax.axis_size(axis)
    pairs = [(i, i + by) for i in range(count) if 0 <= i + by < count]
    return lax.ppermute(value, axis, pairs)


def spread(kernel, pixel, padded_side):
    cell_index = jnp.arange(padded_side, dtype=jnp.int32)[:, None] - pixel[None, :]
    tap_index = jnp.arange(kernel.shape[0], dtype=jnp.int32)[:, None, None]
    return jnp.sum(jnp.where(cell_index[None] == tap_index, kernel[:, None, :], 0.0), axis=0)


def kernel_of(taper, offset):
    levels = jnp.arange(taper.shape[1], dtype=jnp.int32)[:, None]
    select = (levels == offset[None, :]).astype(jnp.float32)
    return jnp.dot(taper, select, precision=lax.Precision.HIGHEST, preferred_element_type=jnp.float32)


def place_rows(spread_u, spread_v, slot_rows):
    weights = (spread_u[:, None, :] * spread_v[None, :, :]).astype(jnp.bfloat16)
    weights = weights.reshape(spread_u.shape[0] * spread_v.shape[0], -1)
    cells = jnp.dot(weights, slot_rows, preferred_element_type=jnp.float32)
    return cells.reshape(spread_u.shape[0], spread_v.shape[0], -1)


def body(visibilities, send_list, pixels, offsets, taper):
    tile_count = lax.axis_size("tile")
    slot_cap = send_list.shape[1]
    rows_dev, components = visibilities.shape
    padded_side = TS + 8
    slot_total = tile_count * slot_cap
    halves = 2
    per_half = slot_cap // halves
    half_lanes = per_half * components + 128

    listed = send_list.transpose(1, 0).reshape(-1)
    row_ids = jnp.arange(rows_dev, dtype=jnp.int32)
    chosen = (listed[:, None] == row_ids[None, :]).astype(jnp.bfloat16)
    outgoing = jnp.dot(chosen, visibilities, preferred_element_type=jnp.float32)
    outgoing = outgoing.astype(jnp.bfloat16)
    meta_src = jnp.concatenate([pixels, offsets], 0).astype(jnp.bfloat16)
    slot_meta = lax.dot_general(
        meta_src, chosen, (((1,), (1,)), ((), ())), preferred_element_type=jnp.float32
    )
    slot_meta = slot_meta.reshape(META, slot_cap, tile_count).transpose(2, 1, 0)
    slot_meta = slot_meta.reshape(tile_count, slot_cap * META).astype(jnp.bfloat16)
    pad = half_lanes - per_half * components
    tails = [
        jnp.pad(slot_meta, ((0, 0), (0, pad - slot_cap * META))),
        jnp.zeros((tile_count, pad), jnp.bfloat16),
    ]
    packed = jnp.stack(
        [
            jnp.concatenate(
                [
                    outgoing[(h * per_half + j) * tile_count : (h * per_half + j + 1) * tile_count]
                    for j in range(per_half)
                ]
                + [tails[h]],
                1,
            )
            for h in range(halves)
        ],
        1,
    )
    arrived = lax.all_to_all(packed, "tile", split_axis=0, concat_axis=0, tiled=True)
    arrived_rows = jnp.concatenate(
        [
            arrived[:, h, j * components : (j + 1) * components]
            for h in range(halves)
            for j in range(per_half)
        ],
        0,
    )
    meta_rows = arrived[:, 0, per_half * components : per_half * components + slot_cap * META]
    meta_rows = meta_rows.astype(jnp.int32).reshape(tile_count, slot_cap, META)
    meta_rows = meta_rows.transpose(2, 1, 0).reshape(META, slot_total)

    spread_u = spread(kernel_of(taper, meta_rows[2]), meta_rows[0], padded_side)
    spread_v = spread(kernel_of(taper, meta_rows[3]), meta_rows[1], padded_side)
    low = place_rows(spread_u[0:4], spread_v, arrived_rows)
    high = place_rows(spread_u[TS + 4 : TS + 7], spread_v, arrived_rows)
    edge_lo = place_rows(spread_u[4 : TS + 4], spread_v[0:4], arrived_rows)
    edge_hi = place_rows(spread_u[4 : TS + 4], spread_v[TS + 4 : TS + 7], arrived_rows)

    tile_row = lax.axis_index("tile") % TILES_Y
    from_below = passed_along(low.astype(jnp.bfloat16), "tile", -TILES_Y)
    from_above = passed_along(high.astype(jnp.bfloat16), "tile", TILES_Y)
    from_next = passed_along(edge_lo, "tile", -1)
    from_prev = passed_along(edge_hi, "tile", 1)
    result = place_rows(spread_u[4 : TS + 4], spread_v[4 : TS + 4], arrived_rows)
    corner_lo = jnp.concatenate([from_below[:, 0:4], from_above[:, 0:4]], 0)
    corner_hi = jnp.concatenate([from_below[:, TS + 4 : TS + 7], from_above[:, TS + 4 : TS + 7]], 0)
    corner_next = passed_along(corner_lo, "tile", -1).astype(jnp.float32)
    corner_prev = passed_along(corner_hi, "tile", 1).astype(jnp.float32)
    has_next = tile_row + 1 < TILES_Y
    has_prev = tile_row >= 1
    from_next = jnp.where(has_next, from_next, 0.0)
    from_prev = jnp.where(has_prev, from_prev, 0.0)
    corner_next = jnp.where(has_next, corner_next, 0.0)
    corner_prev = jnp.where(has_prev, corner_prev, 0.0)
    from_below = from_below[:, 4 : TS + 4].astype(jnp.float32)
    from_above = from_above[:, 4 : TS + 4].astype(jnp.float32)
    result = result.at[TS - 4 : TS].add(from_below)
    result = result.at[0:3].add(from_above)
    result = result.at[:, TS - 4 : TS].add(from_next)
    result = result.at[:, 0:3].add(from_prev)
    result = result.at[TS - 4 : TS, TS - 4 : TS].add(corner_next[0:4])
    result = result.at[0:3, TS - 4 : TS].add(corner_next[4:7])
    result = result.at[TS - 4 : TS, 0:3].add(corner_prev[0:4])
    result = result.at[0:3, 0:3].add(corner_prev[4:7])
    return result[None]


def solution(mesh):
    placed = (
        P("tile", "chan"),
        P(("chan", "tile"), None),
        P(None, ("chan", "tile")),
        P(None, ("chan", "tile")),
        P(),
    )
    return jax.shard_map(
        body, mesh=mesh, in_specs=placed, out_specs=P("tile", None, None, "chan"), check_vma=False
    )
```

```python
import jax
import jax.numpy as jnp
from jax import lax
from jax.sharding import PartitionSpec as P

TS = 32
TILES_Y = 8
META = 4


def passed_along(value, axis, by):
    count = lax.axis_size(axis)
    pairs = [(i, i + by) for i in range(count) if 0 <= i + by < count]
    return lax.ppermute(value, axis, pairs)


def spread(kernel, pixel, padded_side):
    cell_index = jnp.arange(padded_side, dtype=jnp.int32)[:, None] - pixel[None, :]
    tap_index = jnp.arange(kernel.shape[0], dtype=jnp.int32)[:, None, None]
    return jnp.sum(jnp.where(cell_index[None] == tap_index, kernel[:, None, :], 0.0), axis=0)


def kernel_of(taper, offset):
    levels = jnp.arange(taper.shape[1], dtype=jnp.int32)[:, None]
    select = (levels == offset[None, :]).astype(jnp.float32)
    return jnp.dot(taper, select, precision=lax.Precision.HIGHEST, preferred_element_type=jnp.float32)


def place_rows(spread_u, spread_v, slot_rows):
    weights = (spread_u[:, None, :] * spread_v[None, :, :]).astype(jnp.bfloat16)
    weights = weights.reshape(spread_u.shape[0] * spread_v.shape[0], -1)
    cells = jnp.dot(weights, slot_rows, preferred_element_type=jnp.float32)
    return cells.reshape(spread_u.shape[0], spread_v.shape[0], -1)


def body(visibilities, send_list, pixels, offsets, taper):
    tile_count = lax.axis_size("tile")
    slot_cap = send_list.shape[1]
    rows_dev, components = visibilities.shape
    padded_side = TS + 8
    slot_total = tile_count * slot_cap
    halves = 2
    per_half = slot_cap // halves
    half_lanes = per_half * components + 128

    listed = send_list.transpose(1, 0).reshape(-1)
    row_ids = jnp.arange(rows_dev, dtype=jnp.int32)
    chosen = (listed[:, None] == row_ids[None, :]).astype(jnp.bfloat16)
    outgoing = jnp.dot(chosen, visibilities, preferred_element_type=jnp.float32)
    outgoing = outgoing.astype(jnp.bfloat16)
    meta_src = jnp.concatenate([pixels, offsets], 0).astype(jnp.bfloat16)
    slot_meta = lax.dot_general(
        meta_src, chosen, (((1,), (1,)), ((), ())), preferred_element_type=jnp.float32
    )
    slot_meta = slot_meta.reshape(META, slot_cap, tile_count).transpose(2, 1, 0)
    slot_meta = slot_meta.reshape(tile_count, slot_cap * META).astype(jnp.bfloat16)
    pad = half_lanes - per_half * components
    tails = [
        jnp.pad(slot_meta, ((0, 0), (0, pad - slot_cap * META))),
        jnp.zeros((tile_count, pad), jnp.bfloat16),
    ]
    packed = jnp.stack(
        [
            jnp.concatenate(
                [
                    outgoing[(h * per_half + j) * tile_count : (h * per_half + j + 1) * tile_count]
                    for j in range(per_half)
                ]
                + [tails[h]],
                1,
            )
            for h in range(halves)
        ],
        1,
    )
    arrived = lax.all_to_all(packed, "tile", split_axis=0, concat_axis=0, tiled=True)
    arrived_rows = jnp.concatenate(
        [
            arrived[:, h, j * components : (j + 1) * components]
            for h in range(halves)
            for j in range(per_half)
        ],
        0,
    )
    meta_rows = arrived[:, 0, per_half * components : per_half * components + slot_cap * META]
    meta_rows = meta_rows.astype(jnp.int32).reshape(tile_count, slot_cap, META)
    meta_rows = meta_rows.transpose(2, 1, 0).reshape(META, slot_total)

    spread_u = spread(kernel_of(taper, meta_rows[2]), meta_rows[0], padded_side)
    spread_v = spread(kernel_of(taper, meta_rows[3]), meta_rows[1], padded_side)
    low = place_rows(spread_u[0:4], spread_v, arrived_rows)
    high = place_rows(spread_u[TS + 4 : TS + 7], spread_v, arrived_rows)

    from_below = passed_along(low.astype(jnp.bfloat16), "tile", -TILES_Y)
    from_above = passed_along(high.astype(jnp.bfloat16), "tile", TILES_Y)
    inner = place_rows(spread_u[4 : TS + 4], spread_v, arrived_rows)
    inner = inner.at[TS - 4 : TS].add(from_below.astype(jnp.float32))
    inner = inner.at[0:3].add(from_above.astype(jnp.float32))
    tile_row = lax.axis_index("tile") % TILES_Y
    from_next = passed_along(inner[:, 0:4].astype(jnp.bfloat16), "tile", -1)
    from_prev = passed_along(inner[:, TS + 4 : TS + 7].astype(jnp.bfloat16), "tile", 1)
    from_next = jnp.where(tile_row + 1 < TILES_Y, from_next.astype(jnp.float32), 0.0)
    from_prev = jnp.where(tile_row >= 1, from_prev.astype(jnp.float32), 0.0)
    result = inner[:, 4 : TS + 4]
    result = result.at[:, TS - 4 : TS].add(from_next)
    result = result.at[:, 0:3].add(from_prev)
    return result[None]


def solution(mesh):
    placed = (
        P("tile", "chan"),
        P(("chan", "tile"), None),
        P(None, ("chan", "tile")),
        P(None, ("chan", "tile")),
        P(),
    )
    return jax.shard_map(
        body, mesh=mesh, in_specs=placed, out_specs=P("tile", None, None, "chan"), check_vma=False
    )
```

```python
import jax
import jax.numpy as jnp
from jax import lax
from jax.sharding import PartitionSpec as P

TS = 32
TILES_Y = 8
META = 4


def passed_along(value, axis, by):
    count = lax.axis_size(axis)
    pairs = [(i, i + by) for i in range(count) if 0 <= i + by < count]
    return lax.ppermute(value, axis, pairs)


def spread(kernel, pixel, padded_side):
    cell_index = jnp.arange(padded_side, dtype=jnp.int32)[:, None] - pixel[None, :]
    tap_index = jnp.arange(kernel.shape[0], dtype=jnp.int32)[:, None, None]
    return jnp.sum(jnp.where(cell_index[None] == tap_index, kernel[:, None, :], 0.0), axis=0)


def kernel_of(taper, offset):
    levels = jnp.arange(taper.shape[1], dtype=jnp.int32)[:, None]
    select = (levels == offset[None, :]).astype(jnp.float32)
    return jnp.dot(taper, select, precision=lax.Precision.HIGHEST, preferred_element_type=jnp.float32)


def place_rows(spread_u, spread_v, slot_rows):
    weights = (spread_u[:, None, :] * spread_v[None, :, :]).astype(jnp.bfloat16)
    weights = weights.reshape(spread_u.shape[0] * spread_v.shape[0], -1)
    cells = jnp.dot(weights, slot_rows, preferred_element_type=jnp.float32)
    return cells.reshape(spread_u.shape[0], spread_v.shape[0], -1)


def body(visibilities, send_list, pixels, offsets, taper):
    tile_count = lax.axis_size("tile")
    slot_cap = send_list.shape[1]
    rows_dev, components = visibilities.shape
    padded_side = TS + 8
    slot_total = tile_count * slot_cap
    halves = 2
    per_half = slot_cap // halves
    half_lanes = per_half * components + 128

    listed = send_list.transpose(1, 0).reshape(-1)
    row_ids = jnp.arange(rows_dev, dtype=jnp.int32)
    chosen = (listed[:, None] == row_ids[None, :]).astype(jnp.bfloat16)
    outgoing = jnp.dot(chosen, visibilities, preferred_element_type=jnp.float32)
    outgoing = outgoing.astype(jnp.bfloat16)
    meta_src = jnp.concatenate([pixels, offsets], 0).astype(jnp.bfloat16)
    slot_meta = lax.dot_general(
        meta_src, chosen, (((1,), (1,)), ((), ())), preferred_element_type=jnp.float32
    )
    slot_meta = slot_meta.reshape(META, slot_cap, tile_count).transpose(2, 1, 0)
    slot_meta = slot_meta.reshape(tile_count, slot_cap * META).astype(jnp.bfloat16)
    pad = half_lanes - per_half * components
    tails = [
        jnp.pad(slot_meta, ((0, 0), (0, pad - slot_cap * META))),
        jnp.zeros((tile_count, pad), jnp.bfloat16),
    ]
    packed = jnp.stack(
        [
            jnp.concatenate(
                [
                    outgoing[(h * per_half + j) * tile_count : (h * per_half + j + 1) * tile_count]
                    for j in range(per_half)
                ]
                + [tails[h]],
                1,
            )
            for h in range(halves)
        ],
        1,
    )
    arrived = lax.all_to_all(packed, "tile", split_axis=0, concat_axis=0, tiled=True)
    arrived_rows = jnp.concatenate(
        [
            arrived[:, h, j * components : (j + 1) * components]
            for h in range(halves)
            for j in range(per_half)
        ],
        0,
    )
    meta_rows = arrived[:, 0, per_half * components : per_half * components + slot_cap * META]
    meta_rows = meta_rows.astype(jnp.int32).reshape(tile_count, slot_cap, META)
    meta_rows = meta_rows.transpose(2, 1, 0).reshape(META, slot_total)

    spread_u = spread(kernel_of(taper, meta_rows[2]), meta_rows[0], padded_side)
    spread_v = spread(kernel_of(taper, meta_rows[3]), meta_rows[1], padded_side)
    span = spread_u[0 : TS + 7]
    edge_lo = place_rows(span, spread_v[0:4], arrived_rows)
    edge_hi = place_rows(span, spread_v[TS + 4 : TS + 7], arrived_rows)

    tile_row = lax.axis_index("tile") % TILES_Y
    from_next = passed_along(edge_lo, "tile", -1)
    from_prev = passed_along(edge_hi, "tile", 1)
    body_cols = place_rows(span, spread_v[4 : TS + 4], arrived_rows)
    from_next = jnp.where(tile_row + 1 < TILES_Y, from_next, 0.0)
    from_prev = jnp.where(tile_row >= 1, from_prev, 0.0)
    body_cols = body_cols.at[:, TS - 4 : TS].add(from_next)
    body_cols = body_cols.at[:, 0:3].add(from_prev)
    from_below = passed_along(body_cols[0:4].astype(jnp.bfloat16), "tile", -TILES_Y)
    from_above = passed_along(body_cols[TS + 4 : TS + 7].astype(jnp.bfloat16), "tile", TILES_Y)
    result = body_cols[4 : TS + 4]
    result = result.at[TS - 4 : TS].add(from_below.astype(jnp.float32))
    result = result.at[0:3].add(from_above.astype(jnp.float32))
    return result[None]


def solution(mesh):
    placed = (
        P("tile", "chan"),
        P(("chan", "tile"), None),
        P(None, ("chan", "tile")),
        P(None, ("chan", "tile")),
        P(),
    )
    return jax.shard_map(
        body, mesh=mesh, in_specs=placed, out_specs=P("tile", None, None, "chan"), check_vma=False
    )
```

```python
import jax
import jax.numpy as jnp
from jax import lax
from jax.sharding import PartitionSpec as P

TS = 32
TILES_Y = 8
META = 4


def passed_along(value, axis, by):
    count = lax.axis_size(axis)
    pairs = [(i, i + by) for i in range(count) if 0 <= i + by < count]
    return lax.ppermute(value, axis, pairs)


def spread(kernel, pixel, padded_side):
    cell_index = jnp.arange(padded_side, dtype=jnp.int32)[:, None] - pixel[None, :]
    tap_index = jnp.arange(kernel.shape[0], dtype=jnp.int32)[:, None, None]
    return jnp.sum(jnp.where(cell_index[None] == tap_index, kernel[:, None, :], 0.0), axis=0)


def kernel_of(taper, offset):
    levels = jnp.arange(taper.shape[1], dtype=jnp.int32)[:, None]
    select = (levels == offset[None, :]).astype(jnp.float32)
    return jnp.dot(taper, select, precision=lax.Precision.HIGHEST, preferred_element_type=jnp.float32)


def place_rows(spread_u, spread_v, slot_rows):
    weights = (spread_u[:, None, :] * spread_v[None, :, :]).astype(jnp.bfloat16)
    weights = weights.reshape(spread_u.shape[0] * spread_v.shape[0], -1)
    cells = jnp.dot(weights, slot_rows, preferred_element_type=jnp.float32)
    return cells.reshape(spread_u.shape[0], spread_v.shape[0], -1)


def body(visibilities, send_list, pixels, offsets, taper):
    tile_count = lax.axis_size("tile")
    slot_cap = send_list.shape[1]
    rows_dev, components = visibilities.shape
    padded_side = TS + 8
    slot_total = tile_count * slot_cap
    halves = 2
    per_half = slot_cap // halves
    half_lanes = per_half * components + 128

    listed = send_list.transpose(1, 0).reshape(-1)
    row_ids = jnp.arange(rows_dev, dtype=jnp.int32)
    chosen = (listed[:, None] == row_ids[None, :]).astype(jnp.bfloat16)
    outgoing = jnp.dot(chosen, visibilities, preferred_element_type=jnp.float32)
    outgoing = outgoing.astype(jnp.bfloat16)
    meta_src = jnp.concatenate([pixels, offsets], 0).astype(jnp.bfloat16)
    slot_meta = lax.dot_general(
        meta_src, chosen, (((1,), (1,)), ((), ())), preferred_element_type=jnp.float32
    )
    slot_meta = slot_meta.reshape(META, slot_cap, tile_count).transpose(2, 1, 0)
    slot_meta = slot_meta.reshape(tile_count, slot_cap * META).astype(jnp.bfloat16)
    pad = half_lanes - per_half * components
    tails = [
        jnp.pad(slot_meta, ((0, 0), (0, pad - slot_cap * META))),
        jnp.zeros((tile_count, pad), jnp.bfloat16),
    ]
    packed = jnp.stack(
        [
            jnp.concatenate(
                [
                    outgoing[(h * per_half + j) * tile_count : (h * per_half + j + 1) * tile_count]
                    for j in range(per_half)
                ]
                + [tails[h]],
                1,
            )
            for h in range(halves)
        ],
        1,
    )
    arrived = lax.all_to_all(packed, "tile", split_axis=0, concat_axis=0, tiled=True)
    arrived_rows = jnp.concatenate(
        [
            arrived[:, h, j * components : (j + 1) * components]
            for h in range(halves)
            for j in range(per_half)
        ],
        0,
    )
    meta_rows = arrived[:, 0, per_half * components : per_half * components + slot_cap * META]
    meta_rows = meta_rows.astype(jnp.int32).reshape(tile_count, slot_cap, META)
    meta_rows = meta_rows.transpose(2, 1, 0).reshape(META, slot_total)

    spread_u = spread(kernel_of(taper, meta_rows[2]), meta_rows[0], padded_side)
    spread_v = spread(kernel_of(taper, meta_rows[3]), meta_rows[1], padded_side)
    low = place_rows(spread_u[0:4], spread_v, arrived_rows)
    high = place_rows(spread_u[TS + 4 : TS + 7], spread_v, arrived_rows)

    from_below = passed_along(low.astype(jnp.bfloat16), "tile", -TILES_Y)
    from_above = passed_along(high.astype(jnp.bfloat16), "tile", TILES_Y)
    inner = place_rows(spread_u[4 : TS + 4], spread_v, arrived_rows)
    inner = inner.at[TS - 4 : TS].add(from_below.astype(jnp.float32))
    inner = inner.at[0:3].add(from_above.astype(jnp.float32))
    tile_row = lax.axis_index("tile") % TILES_Y
    from_next = passed_along(inner[:, 0:4], "tile", -1)
    from_prev = passed_along(inner[:, TS + 4 : TS + 7], "tile", 1)
    from_next = jnp.where(tile_row + 1 < TILES_Y, from_next, 0.0)
    from_prev = jnp.where(tile_row >= 1, from_prev, 0.0)
    result = (
        inner[:, 4 : TS + 4]
        + jnp.pad(from_next, ((0, 0), (TS - 4, 0), (0, 0)))
        + jnp.pad(from_prev, ((0, 0), (0, TS - 3), (0, 0)))
    )
    return result[None]


def solution(mesh):
    placed = (
        P("tile", "chan"),
        P(("chan", "tile"), None),
        P(None, ("chan", "tile")),
        P(None, ("chan", "tile")),
        P(),
    )
    return jax.shard_map(
        body, mesh=mesh, in_specs=placed, out_specs=P("tile", None, None, "chan"), check_vma=False
    )
```

```python
import jax
import jax.numpy as jnp
from jax import lax
from jax.sharding import PartitionSpec as P

TS = 32
TILES_Y = 8
META = 4


def passed_along(value, axis, by):
    count = lax.axis_size(axis)
    pairs = [(i, i + by) for i in range(count) if 0 <= i + by < count]
    return lax.ppermute(value, axis, pairs)


def spread(kernel, pixel, padded_side):
    cell_index = jnp.arange(padded_side, dtype=jnp.int32)[:, None] - pixel[None, :]
    tap_index = jnp.arange(kernel.shape[0], dtype=jnp.int32)[:, None, None]
    return jnp.sum(jnp.where(cell_index[None] == tap_index, kernel[:, None, :], 0.0), axis=0)


def kernel_of(taper, offset):
    levels = jnp.arange(taper.shape[1], dtype=jnp.int32)[:, None]
    select = (levels == offset[None, :]).astype(jnp.float32)
    return jnp.dot(taper, select, precision=lax.Precision.HIGHEST, preferred_element_type=jnp.float32)


def place_rows(spread_u, spread_v, slot_rows):
    weights = (spread_u[:, None, :] * spread_v[None, :, :]).astype(jnp.bfloat16)
    weights = weights.reshape(spread_u.shape[0] * spread_v.shape[0], -1)
    cells = jnp.dot(weights, slot_rows, preferred_element_type=jnp.float32)
    return cells.reshape(spread_u.shape[0], spread_v.shape[0], -1)


def body(visibilities, send_list, pixels, offsets, taper):
    tile_count = lax.axis_size("tile")
    slot_cap = send_list.shape[1]
    rows_dev, components = visibilities.shape
    padded_side = TS + 8
    slot_total = tile_count * slot_cap
    halves = 2
    per_half = slot_cap // halves
    half_lanes = per_half * components + 128

    listed = send_list.transpose(1, 0).reshape(-1)
    row_ids = jnp.arange(rows_dev, dtype=jnp.int32)
    chosen = (listed[:, None] == row_ids[None, :]).astype(jnp.bfloat16)
    meta_src = jnp.concatenate([pixels, offsets], 0).astype(jnp.bfloat16)
    slot_meta = lax.dot_general(
        meta_src, chosen, (((1,), (1,)), ((), ())), preferred_element_type=jnp.float32
    )
    slot_meta, visibilities = lax.optimization_barrier((slot_meta, visibilities))
    outgoing = jnp.dot(chosen, visibilities, preferred_element_type=jnp.float32)
    outgoing = outgoing.astype(jnp.bfloat16)
    slot_meta = slot_meta.reshape(META, slot_cap, tile_count).transpose(2, 1, 0)
    slot_meta = slot_meta.reshape(tile_count, slot_cap * META).astype(jnp.bfloat16)
    pad = half_lanes - per_half * components
    tails = [
        jnp.pad(slot_meta, ((0, 0), (0, pad - slot_cap * META))),
        jnp.zeros((tile_count, pad), jnp.bfloat16),
    ]
    packed = jnp.stack(
        [
            jnp.concatenate(
                [
                    outgoing[(h * per_half + j) * tile_count : (h * per_half + j + 1) * tile_count]
                    for j in range(per_half)
                ]
                + [tails[h]],
                1,
            )
            for h in range(halves)
        ],
        1,
    )
    arrived = lax.all_to_all(packed, "tile", split_axis=0, concat_axis=0, tiled=True)
    arrived_rows = jnp.concatenate(
        [
            arrived[:, h, j * components : (j + 1) * components]
            for h in range(halves)
            for j in range(per_half)
        ],
        0,
    )
    meta_rows = arrived[:, 0, per_half * components : per_half * components + slot_cap * META]
    meta_rows = meta_rows.astype(jnp.int32).reshape(tile_count, slot_cap, META)
    meta_rows = meta_rows.transpose(2, 1, 0).reshape(META, slot_total)

    spread_u = spread(kernel_of(taper, meta_rows[2]), meta_rows[0], padded_side)
    spread_v = spread(kernel_of(taper, meta_rows[3]), meta_rows[1], padded_side)
    low = place_rows(spread_u[0:4], spread_v, arrived_rows)
    high = place_rows(spread_u[TS + 4 : TS + 7], spread_v, arrived_rows)

    from_below = passed_along(low.astype(jnp.bfloat16), "tile", -TILES_Y)
    from_above = passed_along(high.astype(jnp.bfloat16), "tile", TILES_Y)
    inner = place_rows(spread_u[4 : TS + 4], spread_v, arrived_rows)
    inner = inner.at[TS - 4 : TS].add(from_below.astype(jnp.float32))
    inner = inner.at[0:3].add(from_above.astype(jnp.float32))
    tile_row = lax.axis_index("tile") % TILES_Y
    from_next = passed_along(inner[:, 0:4], "tile", -1)
    from_prev = passed_along(inner[:, TS + 4 : TS + 7], "tile", 1)
    from_next = jnp.where(tile_row + 1 < TILES_Y, from_next, 0.0)
    from_prev = jnp.where(tile_row >= 1, from_prev, 0.0)
    result = (
        inner[:, 4 : TS + 4]
        + jnp.pad(from_next, ((0, 0), (TS - 4, 0), (0, 0)))
        + jnp.pad(from_prev, ((0, 0), (0, TS - 3), (0, 0)))
    )
    return result[None]


def solution(mesh):
    placed = (
        P("tile", "chan"),
        P(("chan", "tile"), None),
        P(None, ("chan", "tile")),
        P(None, ("chan", "tile")),
        P(),
    )
    return jax.shard_map(
        body, mesh=mesh, in_specs=placed, out_specs=P("tile", None, None, "chan"), check_vma=False
    )
```
